256 devices in a mesh: dp: 16 (over z_lo, y, core), ctx: 16 (over x, z_hi).
Axes of the slice: x: 4, y: 4, z: 8 (z_hi: 4, z_lo: 2; z = z_hi * 2 + z_lo), core: 2. Of those that a mesh axis runs over, the one named last changes fastest.
Arguments:
- tokens: bfloat16 [16, 2048, 2560], P('dp', 'ctx'), may hold values from -6 to 6
- shard_counts: int32 [16, 16], P('dp'), may hold values from 64 to 128, as said below
- stretch_start: int32 [16], P('dp'), may hold values from 102 to 409, as said below
- segment_ids: int32 [16, 2048], P('dp', 'ctx'), may hold values from 0 to 1, as said below
- span_ids: int32 [16, 2048], P('dp', 'ctx'), may hold values from -1 to 31, as said below
- query_weight: bfloat16 [2560, 2560], P('dp'), may hold values from -0.125 to 0.125
- key_matrix: bfloat16 [2560, 512], P('dp'), may hold values from -0.125 to 0.125
- value_matrix: bfloat16 [2560, 512], P('dp'), may hold values from -0.125 to 0.125
- score_vector: bfloat16 [2560], replicated, may hold values from -4 to 4
Outputs:
- attention: bfloat16 [16, 2048, 2560], P('dp', 'ctx')
- candidate_loglik: float32 [16, 32], P('dp')
The draws below stay inside these ranges and needn't reach their ends.
Inputs may be any that keep to these rules, and one draw needn't show every extreme that they name: `shard_counts`: in every sequence at least one shard has exactly 128 live tokens. `stretch_start`: A stretch of each sequence starts at a position held by one of its live tokens, after the first. `segment_ids`: along the live tokens of a sequence, segment ids never fall. `span_ids`: each candidate of every sequence covers one or more live tokens, in one run of consecutive positions; empty slots have -1.
All inputs are finite; a program needn't handle non-finite values.
Results may differ from the reference program's by a relative error of at most 0.0066.
Values may be sent and summed in bfloat16 or wider, within the bound.
No kernel may reach another device: no remote copies, remote signals or barrier semaphores. Data moves between devices by JAX's collectives and lax.ppermute only.
A program may use at most 128 MiB of HBM per device.

```python
import math
import jax
import jax.numpy as jnp
from jax import lax

MODEL_FEATURES = 2560
QUERY_HEADS = 20
KEY_VALUE_HEADS = 4
HEAD_SIZE = 128
STRETCH = 8192
SHARD_SLOTS = 128
CAND = 32
ROWS = 2048
SEQS = 16
N_DP = 16
N_CTX = 16


def layout(key):
    counts = jax.random.randint(jax.random.fold_in(key, 101), (N_DP, N_CTX), SHARD_SLOTS // 2, SHARD_SLOTS + 1)
    fullest = jax.random.randint(jax.random.fold_in(key, 102), (N_DP, 1), 0, N_CTX)
    counts = jnp.where(jnp.arange(N_CTX)[None, :] == fullest, SHARD_SLOTS, counts).astype(jnp.int32)
    total = jnp.sum(counts, axis=1)
    starts = jnp.cumsum(counts, axis=1) - counts
    offsets = jnp.arange(SHARD_SLOTS, dtype=jnp.int32)
    token_places = starts[:, :, None] + offsets[None, None, :]
    live = offsets[None, None, :] < counts[:, :, None]
    doc_pick = jax.random.randint(jax.random.fold_in(key, 103), (N_DP,), 0, 151)
    stretch_pick = jax.random.randint(jax.random.fold_in(key, 104), (N_DP,), 0, 151)
    seq_order = jnp.arange(N_DP, dtype=jnp.int32)
    stretch_pick = jnp.where(seq_order == 0, 150, jnp.where(seq_order == 1, 0, stretch_pick))
    doc_edge = total * (750 + doc_pick) // 1000
    stretch_edge = N_CTX * SHARD_SLOTS * (50 + stretch_pick) // 1000
    segs = (token_places >= doc_edge[:, None, None]).astype(jnp.int32).reshape(N_DP, N_CTX * SHARD_SLOTS)
    region = total // CAND
    slot = token_places // region[:, None, None]
    within = token_places - slot * region[:, None, None]
    quarter = region[:, None] // 4
    lengths = quarter + jax.random.randint(jax.random.fold_in(key, 105), (N_DP, CAND), 0, 1 << 20) % (quarter + 1)
    picked = jnp.take_along_axis(lengths, jnp.minimum(slot, CAND - 1).reshape(N_DP, N_CTX * SHARD_SLOTS), axis=1).reshape(N_DP, N_CTX, SHARD_SLOTS)
    chosen = live & (slot < CAND) & (within >= region[:, None, None] - picked)
    spans = jnp.where(chosen, slot, -1).astype(jnp.int32).reshape(N_DP, N_CTX * SHARD_SLOTS)
    return (counts, stretch_edge.astype(jnp.int32), segs, spans)


def draw_shard_counts(key, part):
    return layout(key)[0]


def draw_stretch_start(key, part):
    return layout(key)[1]


def draw_segment_ids(key, part):
    return layout(key)[2]


def draw_span_ids(key, part):
    return layout(key)[3]


def block_scale(key, extent, pieces, low, high):
    def one(position, blocks):
        steps = jax.random.uniform(jax.random.fold_in(jax.random.fold_in(key, 6), position), (blocks,), jnp.float32, low / len(pieces), high / len(pieces))
        return jnp.repeat(jnp.exp(steps), extent[position] // blocks).reshape((-1,) + (1,) * (len(extent) - position - 1))

    gain = one(*pieces[0])
    for cut in pieces[1:]:
        gain = gain * one(*cut)
    return gain


def bell_draw(key, extent, scale, bound, split=(), kind=jnp.bfloat16):
    values = jax.random.normal(key, extent, jnp.float32) * scale
    if len(split) > 0:
        values = block_scale(key, extent, split, -0.22, 0.18) * values
    return jnp.clip(values, min=-bound, max=bound).astype(kind)


def setup_inputs(seed: int = 0) -> dict:
    key_of = jax.random.split(jax.random.key(seed), 10)
    return {
        "tokens": bell_draw(key_of[0], (SEQS, ROWS, MODEL_FEATURES), 1.0, 6.0, ((0, 16), (1, 16))),
        "shard_counts": draw_shard_counts(jax.random.fold_in(key_of[9], 71), 0),
        "stretch_start": draw_stretch_start(jax.random.fold_in(key_of[9], 71), 0),
        "segment_ids": draw_segment_ids(jax.random.fold_in(key_of[9], 71), 0),
        "span_ids": draw_span_ids(jax.random.fold_in(key_of[9], 71), 0),
        "query_weight": bell_draw(key_of[5], (MODEL_FEATURES, QUERY_HEADS * HEAD_SIZE), MODEL_FEATURES ** -0.5, 0.125, ((0, 16),)),
        "key_matrix": bell_draw(key_of[6], (MODEL_FEATURES, KEY_VALUE_HEADS * HEAD_SIZE), MODEL_FEATURES ** -0.5, 0.125, ((0, 16),)),
        "value_matrix": bell_draw(key_of[7], (MODEL_FEATURES, KEY_VALUE_HEADS * HEAD_SIZE), MODEL_FEATURES ** -0.5, 0.125, ((0, 16),)),
        "score_vector": bell_draw(key_of[8], (QUERY_HEADS * HEAD_SIZE,), 1.0, 4.0),
    }


THETA = 500000.0
EPS = 1e-05

def rotary_then_norm(value_rows, token_places, heads):
    token_count = value_rows.shape[0]
    half = HEAD_SIZE // 2
    shaped = value_rows.reshape(token_count, heads, HEAD_SIZE)
    freqs = jnp.exp(jnp.arange(half, dtype=jnp.float32) * (-2.0 * math.log(THETA) / HEAD_SIZE))
    angles = token_places.astype(jnp.float32)[:, None] * freqs[None, :]
    cosine = jnp.cos(angles)[:, None, :]
    sine = jnp.sin(angles)[:, None, :]
    leading_block = shaped[..., :half]
    second = shaped[..., half:]
    turned = jnp.concatenate([leading_block * cosine - second * sine, second * cosine + leading_block * sine], axis=-1)
    scale = lax.rsqrt(lax.optimization_barrier(jnp.mean(turned * turned, axis=-1, keepdims=True)) + EPS)
    return (turned * scale).astype(jnp.bfloat16).reshape(token_count, heads * HEAD_SIZE)

def one_sequence(tokens, counts, cstart, segs, spans, query_weight, key_matrix, value_matrix, score_vector):
    row_total = N_CTX * SHARD_SLOTS
    starts = jnp.cumsum(counts) - counts
    offsets = jnp.arange(SHARD_SLOTS, dtype=jnp.int32)
    token_places = (starts[:, None] + offsets[None, :]).reshape(row_total).astype(jnp.int32)
    live = (offsets[None, :] < counts[:, None]).reshape(row_total)
    query = jnp.dot(tokens, query_weight, preferred_element_type=jnp.float32)
    key_rows = jnp.dot(tokens, key_matrix, preferred_element_type=jnp.float32)
    value_rows = jnp.dot(tokens, value_matrix, preferred_element_type=jnp.float32).astype(jnp.bfloat16)
    query_norm = rotary_then_norm(query, token_places, QUERY_HEADS)
    key_norm = rotary_then_norm(key_rows, token_places, KEY_VALUE_HEADS)
    stretch = (token_places + STRETCH - cstart) // STRETCH
    kplace = jnp.where(live, token_places + 1, 0).astype(jnp.int32)
    head_group = QUERY_HEADS // KEY_VALUE_HEADS
    per_head_keys = key_norm.astype(jnp.float32).reshape(row_total, KEY_VALUE_HEADS, HEAD_SIZE)
    per_head_values = value_rows.astype(jnp.float32).reshape(row_total, KEY_VALUE_HEADS, HEAD_SIZE)

    def block(index):
        leading_block = (index * SHARD_SLOTS).astype(jnp.int32)
        query_portion = lax.dynamic_slice_in_dim(query_norm, leading_block, SHARD_SLOTS, 0).astype(jnp.float32).reshape(SHARD_SLOTS, KEY_VALUE_HEADS, head_group, HEAD_SIZE)
        qplace = lax.dynamic_slice_in_dim(token_places, leading_block, SHARD_SLOTS, 0)
        qseg = lax.dynamic_slice_in_dim(segs, leading_block, SHARD_SLOTS, 0)
        qchunk = lax.dynamic_slice_in_dim(stretch, leading_block, SHARD_SLOTS, 0)
        qlive = lax.dynamic_slice_in_dim(live, leading_block, SHARD_SLOTS, 0)
        scores = jnp.einsum('qhgd,khd->hgqk', query_portion, per_head_keys) * (1.0 / math.sqrt(HEAD_SIZE))
        allowed = (segs[None, :] == qseg[:, None]) & (stretch[None, :] == qchunk[:, None])
        allowed = allowed & (kplace[None, :] >= 1) & (kplace[None, :] <= qplace[:, None] + 1)
        weights = jnp.where(allowed[None, None], jnp.exp(scores), 0.0)
        denom = jnp.transpose(lax.optimization_barrier(jnp.sum(weights, axis=-1)), (2, 0, 1))
        numer = jnp.einsum('hgqk,khd->qhgd', weights.astype(jnp.bfloat16).astype(jnp.float32), per_head_values)
        safe = jnp.where(qlive[:, None, None], denom, 1.0)
        result = numer / safe[..., None] * qlive[:, None, None, None].astype(jnp.float32)
        return result.reshape(SHARD_SLOTS, QUERY_HEADS * HEAD_SIZE).astype(jnp.bfloat16)
    attention = lax.map(block, jnp.arange(N_CTX, dtype=jnp.int32)).reshape(row_total, QUERY_HEADS * HEAD_SIZE)
    verdict = jnp.dot(attention, score_vector, preferred_element_type=jnp.float32)
    loglik = jax.nn.log_sigmoid(verdict)
    onehot = spans[:, None] == jnp.arange(CAND, dtype=jnp.int32)[None, :]
    sums = lax.optimization_barrier(jnp.sum(jnp.where(onehot, loglik[:, None], 0.0), axis=0))
    tally = lax.optimization_barrier(jnp.sum(onehot.astype(jnp.float32), axis=0))
    return (attention, sums / tally)

def reference(tokens, shard_counts, stretch_start, segment_ids, span_ids, query_weight, key_matrix, value_matrix, score_vector):

    def per_sequence(items):
        return one_sequence(items[0], items[1], items[2], items[3], items[4], query_weight, key_matrix, value_matrix, score_vector)
    attention, candidate_loglik = lax.map(per_sequence, (tokens, shard_counts, stretch_start, segment_ids, span_ids))
    return (attention, candidate_loglik)
```

```python
import math

import jax
import jax.numpy as jnp
from jax import lax
from jax.sharding import PartitionSpec as P

QUERY_HEADS = 20
KEY_VALUE_HEADS = 4
HEAD_SIZE = 128
STRETCH = 8192
CAND = 32


THETA = 500000.0
EPS = 1e-05


def rotary_then_norm(value_rows, token_places, heads):
    token_count = value_rows.shape[0]
    half = HEAD_SIZE // 2
    shaped = value_rows.reshape(token_count, heads, HEAD_SIZE)
    freqs = jnp.exp(jnp.arange(half, dtype=jnp.float32) * (-2.0 * math.log(THETA) / HEAD_SIZE))
    angles = token_places.astype(jnp.float32)[:, None] * freqs[None, :]
    cosine = jnp.cos(angles)[:, None, :]
    sine = jnp.sin(angles)[:, None, :]
    leading_block = shaped[..., :half]
    second = shaped[..., half:]
    turned = jnp.concatenate(
        [leading_block * cosine - second * sine, second * cosine + leading_block * sine], axis=-1
    )
    scale = lax.rsqrt(jnp.mean(turned * turned, axis=-1, keepdims=True) + EPS)
    return (turned * scale).astype(jnp.bfloat16).reshape(token_count, heads * HEAD_SIZE)


def make_per_device(shards):
    def per_device(
        tokens,
        shard_counts,
        stretch_start,
        segment_ids,
        span_ids,
        query_weight,
        key_matrix,
        value_matrix,
        score_vector,
    ):
        inputs = tokens[0]
        token_slots = inputs.shape[0]
        kv_width = KEY_VALUE_HEADS * HEAD_SIZE
        mine = lax.axis_index("ctx")
        counts = shard_counts[0]
        starts = jnp.cumsum(counts) - counts
        offsets = jnp.arange(token_slots, dtype=jnp.int32)
        token_places = starts[mine] + offsets
        live = offsets < counts[mine]
        cstart = stretch_start[0]
        qseg = segment_ids[0]
        qchunk = (token_places + STRETCH - cstart) // STRETCH

        kv_weights = lax.all_gather(
            jnp.concatenate([key_matrix, value_matrix], axis=1), "dp", axis=0, tiled=True
        )
        kv_rows = jnp.dot(inputs, kv_weights, preferred_element_type=jnp.float32)
        key_norm = rotary_then_norm(kv_rows[:, :kv_width], token_places, KEY_VALUE_HEADS)
        value_rows = kv_rows[:, kv_width:].astype(jnp.bfloat16)
        seg_row = jnp.zeros((8, 2 * kv_width), jnp.bfloat16)
        seg_row = seg_row.at[0, :token_slots].set(qseg.astype(jnp.bfloat16))
        own_block = jnp.concatenate(
            [jnp.concatenate([key_norm, value_rows], axis=1), seg_row], axis=0
        )
        blocks = [own_block]
        for shift in range(1, shards):
            pairs = [(s, s + shift) for s in range(shards - shift)]
            blocks.append(lax.ppermute(own_block, "ctx", pairs))

        query_weights = lax.all_gather(query_weight, "dp", axis=0, tiled=True)
        query = jnp.dot(inputs, query_weights, preferred_element_type=jnp.float32)
        query_norm = rotary_then_norm(query, token_places, QUERY_HEADS)
        head_group = QUERY_HEADS // KEY_VALUE_HEADS
        per_head_queries = query_norm.reshape(token_slots, KEY_VALUE_HEADS, head_group, HEAD_SIZE)

        numer = jnp.zeros((token_slots, KEY_VALUE_HEADS, head_group, HEAD_SIZE), jnp.float32)
        denom = jnp.zeros((KEY_VALUE_HEADS, head_group, token_slots), jnp.float32)
        for shift, block in enumerate(blocks):
            source = mine - shift
            present = source >= 0
            source = jnp.maximum(source, 0)
            kpos = starts[source] + offsets
            klive = (offsets < counts[source]) & present
            kchunk = (kpos + STRETCH - cstart) // STRETCH
            kseg = block[token_slots, :token_slots].astype(jnp.int32)
            key_portion = block[:token_slots, :kv_width].reshape(
                token_slots, KEY_VALUE_HEADS, HEAD_SIZE
            )
            value_portion = block[:token_slots, kv_width:].reshape(
                token_slots, KEY_VALUE_HEADS, HEAD_SIZE
            )
            scores = jnp.einsum(
                "qhgd,khd->hgqk",
                per_head_queries,
                key_portion,
                preferred_element_type=jnp.float32,
            ) * (1.0 / math.sqrt(HEAD_SIZE))
            allowed = (kseg[None, :] == qseg[:, None]) & (kchunk[None, :] == qchunk[:, None])
            allowed = allowed & klive[None, :] & (kpos[None, :] <= token_places[:, None])
            weights = jnp.where(allowed[None, None], jnp.exp(scores), 0.0)
            denom = denom + jnp.sum(weights, axis=-1)
            numer = numer + jnp.einsum(
                "hgqk,khd->qhgd",
                weights.astype(jnp.bfloat16),
                value_portion,
                preferred_element_type=jnp.float32,
            )

        denom_rows = jnp.transpose(denom, (2, 0, 1))
        safe = jnp.where(live[:, None, None], denom_rows, 1.0)
        result = numer / safe[..., None] * live[:, None, None, None].astype(jnp.float32)
        attention = result.reshape(token_slots, QUERY_HEADS * HEAD_SIZE).astype(jnp.bfloat16)
        verdict = jnp.dot(attention, score_vector, preferred_element_type=jnp.float32)
        loglik = jax.nn.log_sigmoid(verdict)
        onehot = span_ids[0][:, None] == jnp.arange(CAND, dtype=jnp.int32)[None, :]
        sums = jnp.sum(jnp.where(onehot, loglik[:, None], 0.0), axis=0)
        tally = jnp.sum(onehot.astype(jnp.float32), axis=0)
        partial = jnp.concatenate([sums, tally])
        gathered = [partial]
        for shift in range(1, shards):
            pairs = [(s, (s + shift) % shards) for s in range(shards)]
            gathered.append(lax.ppermute(partial, "ctx", pairs))
        stacked = jnp.stack(gathered)
        order = (mine - jnp.arange(shards, dtype=jnp.int32)) % shards
        total = jnp.sum(jnp.take(stacked, order, axis=0), axis=0)
        return (attention[None], (total[:CAND] / total[CAND:])[None])

    return per_device


def solution(mesh):
    placed = (
        P("dp", "ctx", None),
        P("dp", None),
        P("dp"),
        P("dp", "ctx"),
        P("dp", "ctx"),
        P("dp", None),
        P("dp", None),
        P("dp", None),
        P(),
    )
    return jax.shard_map(
        make_per_device(mesh.shape["ctx"]),
        mesh=mesh,
        in_specs=placed,
        out_specs=(P("dp", "ctx", None), P("dp", None)),
        check_vma=False,
    )
```

```python
import math

import jax
import jax.numpy as jnp
from jax import lax
from jax.sharding import PartitionSpec as P

QUERY_HEADS = 20
KEY_VALUE_HEADS = 4
HEAD_SIZE = 128
STRETCH = 8192
CAND = 32


THETA = 500000.0
EPS = 1e-05


def rotary_then_norm(value_rows, token_places, heads):
    token_count = value_rows.shape[0]
    half = HEAD_SIZE // 2
    shaped = value_rows.reshape(token_count, heads, HEAD_SIZE)
    freqs = jnp.exp(jnp.arange(half, dtype=jnp.float32) * (-2.0 * math.log(THETA) / HEAD_SIZE))
    angles = token_places.astype(jnp.float32)[:, None] * freqs[None, :]
    cosine = jnp.cos(angles)[:, None, :]
    sine = jnp.sin(angles)[:, None, :]
    leading_block = shaped[..., :half]
    second = shaped[..., half:]
    turned = jnp.concatenate(
        [leading_block * cosine - second * sine, second * cosine + leading_block * sine], axis=-1
    )
    scale = lax.rsqrt(jnp.mean(turned * turned, axis=-1, keepdims=True) + EPS)
    return (turned * scale).astype(jnp.bfloat16).reshape(token_count, heads * HEAD_SIZE)


def make_per_device(shards):
    def per_device(
        tokens,
        shard_counts,
        stretch_start,
        segment_ids,
        span_ids,
        query_weight,
        key_matrix,
        value_matrix,
        score_vector,
    ):
        inputs = tokens[0]
        token_slots = inputs.shape[0]
        kv_width = KEY_VALUE_HEADS * HEAD_SIZE
        mine = lax.axis_index("ctx")
        counts = shard_counts[0]
        starts = jnp.cumsum(counts) - counts
        offsets = jnp.arange(token_slots, dtype=jnp.int32)
        token_places = starts[mine] + offsets
        live = offsets < counts[mine]
        cstart = stretch_start[0]
        qseg = segment_ids[0]
        qchunk = (token_places + STRETCH - cstart) // STRETCH

        kv_weights = lax.all_gather(
            jnp.concatenate([key_matrix, value_matrix], axis=1), "dp", axis=0, tiled=True
        )
        kv_rows = jnp.dot(inputs, kv_weights, preferred_element_type=jnp.float32)
        key_norm = rotary_then_norm(kv_rows[:, :kv_width], token_places, KEY_VALUE_HEADS)
        value_rows = kv_rows[:, kv_width:].astype(jnp.bfloat16)
        seg_row = jnp.zeros((8, 2 * kv_width), jnp.bfloat16)
        seg_row = seg_row.at[0, :token_slots].set(qseg.astype(jnp.bfloat16))
        own_block = jnp.concatenate(
            [jnp.concatenate([key_norm, value_rows], axis=1), seg_row], axis=0
        )
        gathered = lax.all_gather(own_block, "ctx", axis=0, tiled=True).reshape(
            shards, token_slots + 8, 2 * kv_width
        )
        key_count = shards * token_slots
        key_portion = gathered[:, :token_slots, :kv_width].reshape(
            key_count, KEY_VALUE_HEADS, HEAD_SIZE
        )
        value_portion = gathered[:, :token_slots, kv_width:].reshape(
            key_count, KEY_VALUE_HEADS, HEAD_SIZE
        )
        kseg = gathered[:, token_slots, :token_slots].reshape(key_count).astype(jnp.int32)
        kpos = (starts[:, None] + offsets[None, :]).reshape(key_count)
        klive = (offsets[None, :] < counts[:, None]).reshape(key_count)
        kchunk = (kpos + STRETCH - cstart) // STRETCH

        query_weights = lax.all_gather(query_weight, "dp", axis=0, tiled=True)
        query = jnp.dot(inputs, query_weights, preferred_element_type=jnp.float32)
        query_norm = rotary_then_norm(query, token_places, QUERY_HEADS)
        head_group = QUERY_HEADS // KEY_VALUE_HEADS
        per_head_queries = query_norm.reshape(token_slots, KEY_VALUE_HEADS, head_group, HEAD_SIZE)

        scores = jnp.einsum(
            "qhgd,khd->hgqk",
            per_head_queries,
            key_portion,
            preferred_element_type=jnp.float32,
        ) * (1.0 / math.sqrt(HEAD_SIZE))
        allowed = (kseg[None, :] == qseg[:, None]) & (kchunk[None, :] == qchunk[:, None])
        allowed = allowed & klive[None, :] & (kpos[None, :] <= token_places[:, None])
        weights = jnp.where(allowed[None, None], jnp.exp(scores), 0.0)
        denom = jnp.sum(weights, axis=-1)
        numer = jnp.einsum(
            "hgqk,khd->qhgd",
            weights.astype(jnp.bfloat16),
            value_portion,
            preferred_element_type=jnp.float32,
        )

        denom_rows = jnp.transpose(denom, (2, 0, 1))
        safe = jnp.where(live[:, None, None], denom_rows, 1.0)
        result = numer / safe[..., None] * live[:, None, None, None].astype(jnp.float32)
        attention = result.reshape(token_slots, QUERY_HEADS * HEAD_SIZE).astype(jnp.bfloat16)
        verdict = jnp.dot(attention, score_vector, preferred_element_type=jnp.float32)
        loglik = jax.nn.log_sigmoid(verdict)
        onehot = span_ids[0][:, None] == jnp.arange(CAND, dtype=jnp.int32)[None, :]
        sums = jnp.sum(jnp.where(onehot, loglik[:, None], 0.0), axis=0)
        tally = jnp.sum(onehot.astype(jnp.float32), axis=0)
        sums, tally = lax.psum((sums, tally), "ctx")
        return (attention[None], (sums / tally)[None])

    return per_device


def solution(mesh):
    placed = (
        P("dp", "ctx", None),
        P("dp", None),
        P("dp"),
        P("dp", "ctx"),
        P("dp", "ctx"),
        P("dp", None),
        P("dp", None),
        P("dp", None),
        P(),
    )
    return jax.shard_map(
        make_per_device(mesh.shape["ctx"]),
        mesh=mesh,
        in_specs=placed,
        out_specs=(P("dp", "ctx", None), P("dp", None)),
        check_vma=False,
    )
```

```python
import math

import jax
import jax.numpy as jnp
from jax import lax
from jax.sharding import PartitionSpec as P

QUERY_HEADS = 20
KEY_VALUE_HEADS = 4
HEAD_SIZE = 128
STRETCH = 8192
CAND = 32


THETA = 500000.0
EPS = 1e-05


def rotary_then_norm(value_rows, token_places, heads):
    token_count = value_rows.shape[0]
    half = HEAD_SIZE // 2
    shaped = value_rows.reshape(token_count, heads, HEAD_SIZE)
    freqs = jnp.exp(jnp.arange(half, dtype=jnp.float32) * (-2.0 * math.log(THETA) / HEAD_SIZE))
    angles = token_places.astype(jnp.float32)[:, None] * freqs[None, :]
    cosine = jnp.cos(angles)[:, None, :]
    sine = jnp.sin(angles)[:, None, :]
    leading_block = shaped[..., :half]
    second = shaped[..., half:]
    turned = jnp.concatenate(
        [leading_block * cosine - second * sine, second * cosine + leading_block * sine], axis=-1
    )
    scale = lax.rsqrt(jnp.mean(turned * turned, axis=-1, keepdims=True) + EPS)
    return (turned * scale).astype(jnp.bfloat16).reshape(token_count, heads * HEAD_SIZE)


def make_per_device(shards):
    def per_device(
        tokens,
        shard_counts,
        stretch_start,
        segment_ids,
        span_ids,
        query_weight,
        key_matrix,
        value_matrix,
        score_vector,
    ):
        inputs = tokens[0]
        token_slots = inputs.shape[0]
        kv_width = KEY_VALUE_HEADS * HEAD_SIZE
        mine = lax.axis_index("ctx")
        counts = shard_counts[0]
        starts = jnp.cumsum(counts) - counts
        offsets = jnp.arange(token_slots, dtype=jnp.int32)
        token_places = starts[mine] + offsets
        live = offsets < counts[mine]
        cstart = stretch_start[0]
        qseg = segment_ids[0]
        qchunk = (token_places + STRETCH - cstart) // STRETCH

        kv_weights = lax.all_gather(
            jnp.concatenate([key_matrix, value_matrix], axis=1), "dp", axis=0, tiled=True
        )
        kv_rows = jnp.dot(inputs, kv_weights, preferred_element_type=jnp.float32)
        key_norm = rotary_then_norm(kv_rows[:, :kv_width], token_places, KEY_VALUE_HEADS)
        value_rows = kv_rows[:, kv_width:].astype(jnp.bfloat16)
        seg_row = jnp.zeros((8, 2 * kv_width), jnp.bfloat16)
        seg_row = seg_row.at[0, :token_slots].set(qseg.astype(jnp.bfloat16))
        own_block = jnp.concatenate(
            [jnp.concatenate([key_norm, value_rows], axis=1), seg_row], axis=0
        )
        query_weights = lax.all_gather(query_weight, "dp", axis=0, tiled=True)
        own_block, query_weights = lax.optimization_barrier((own_block, query_weights))
        query = jnp.dot(inputs, query_weights, preferred_element_type=jnp.float32)
        gathered = lax.all_gather(own_block, "ctx", axis=0, tiled=True).reshape(
            shards, token_slots + 8, 2 * kv_width
        )
        key_count = shards * token_slots
        key_portion = gathered[:, :token_slots, :kv_width].reshape(
            key_count, KEY_VALUE_HEADS, HEAD_SIZE
        )
        value_portion = gathered[:, :token_slots, kv_width:].reshape(
            key_count, KEY_VALUE_HEADS, HEAD_SIZE
        )
        kseg = gathered[:, token_slots, :token_slots].reshape(key_count).astype(jnp.int32)
        kpos = (starts[:, None] + offsets[None, :]).reshape(key_count)
        klive = (offsets[None, :] < counts[:, None]).reshape(key_count)
        kchunk = (kpos + STRETCH - cstart) // STRETCH

        query_norm = rotary_then_norm(query, token_places, QUERY_HEADS)
        head_group = QUERY_HEADS // KEY_VALUE_HEADS
        per_head_queries = query_norm.reshape(token_slots, KEY_VALUE_HEADS, head_group, HEAD_SIZE)

        scores = jnp.einsum(
            "qhgd,khd->hgqk",
            per_head_queries,
            key_portion,
            preferred_element_type=jnp.float32,
        ) * (1.0 / math.sqrt(HEAD_SIZE))
        allowed = (kseg[None, :] == qseg[:, None]) & (kchunk[None, :] == qchunk[:, None])
        allowed = allowed & klive[None, :] & (kpos[None, :] <= token_places[:, None])
        weights = jnp.where(allowed[None, None], jnp.exp(scores), 0.0)
        denom = jnp.sum(weights, axis=-1)
        numer = jnp.einsum(
            "hgqk,khd->qhgd",
            weights.astype(jnp.bfloat16),
            value_portion,
            preferred_element_type=jnp.float32,
        )

        denom_rows = jnp.transpose(denom, (2, 0, 1))
        safe = jnp.where(live[:, None, None], denom_rows, 1.0)
        result = numer / safe[..., None] * live[:, None, None, None].astype(jnp.float32)
        attention = result.reshape(token_slots, QUERY_HEADS * HEAD_SIZE).astype(jnp.bfloat16)
        verdict = jnp.dot(attention, score_vector, preferred_element_type=jnp.float32)
        loglik = jax.nn.log_sigmoid(verdict)
        onehot = span_ids[0][:, None] == jnp.arange(CAND, dtype=jnp.int32)[None, :]
        sums = jnp.sum(jnp.where(onehot, loglik[:, None], 0.0), axis=0)
        tally = jnp.sum(onehot.astype(jnp.float32), axis=0)
        sums, tally = lax.psum((sums, tally), "ctx")
        return (attention[None], (sums / tally)[None])

    return per_device


def solution(mesh):
    placed = (
        P("dp", "ctx", None),
        P("dp", None),
        P("dp"),
        P("dp", "ctx"),
        P("dp", "ctx"),
        P("dp", None),
        P("dp", None),
        P("dp", None),
        P(),
    )
    return jax.shard_map(
        make_per_device(mesh.shape["ctx"]),
        mesh=mesh,
        in_specs=placed,
        out_specs=(P("dp", "ctx", None), P("dp", None)),
        check_vma=False,
    )
```

```python
import math

import jax
import jax.numpy as jnp
from jax import lax
from jax.sharding import PartitionSpec as P

QUERY_HEADS = 20
KEY_VALUE_HEADS = 4
HEAD_SIZE = 128
STRETCH = 8192
CAND = 32


THETA = 500000.0
EPS = 1e-05


def rotary_then_norm(value_rows, token_places, heads):
    token_count = value_rows.shape[0]
    half = HEAD_SIZE // 2
    shaped = value_rows.reshape(token_count, heads, HEAD_SIZE)
    freqs = jnp.exp(jnp.arange(half, dtype=jnp.float32) * (-2.0 * math.log(THETA) / HEAD_SIZE))
    angles = token_places.astype(jnp.float32)[:, None] * freqs[None, :]
    cosine = jnp.cos(angles)[:, None, :]
    sine = jnp.sin(angles)[:, None, :]
    leading_block = shaped[..., :half]
    second = shaped[..., half:]
    turned = jnp.concatenate(
        [leading_block * cosine - second * sine, second * cosine + leading_block * sine], axis=-1
    )
    scale = lax.rsqrt(jnp.mean(turned * turned, axis=-1, keepdims=True) + EPS)
    return (turned * scale).astype(jnp.bfloat16).reshape(token_count, heads * HEAD_SIZE)


def make_per_device(shards):
    def per_device(
        tokens,
        shard_counts,
        stretch_start,
        segment_ids,
        span_ids,
        query_weight,
        key_matrix,
        value_matrix,
        score_vector,
    ):
        inputs = tokens[0]
        token_slots = inputs.shape[0]
        kv_width = KEY_VALUE_HEADS * HEAD_SIZE
        mine = lax.axis_index("ctx")
        counts = shard_counts[0]
        starts = jnp.cumsum(counts) - counts
        offsets = jnp.arange(token_slots, dtype=jnp.int32)
        token_places = starts[mine] + offsets
        live = offsets < counts[mine]
        cstart = stretch_start[0]
        qseg = segment_ids[0]
        qchunk = (token_places + STRETCH - cstart) // STRETCH

        kv_weights = lax.all_gather(
            jnp.concatenate([key_matrix, value_matrix], axis=1), "dp", axis=0, tiled=True
        )
        kv_rows = jnp.dot(inputs, kv_weights, preferred_element_type=jnp.float32)
        key_norm = rotary_then_norm(kv_rows[:, :kv_width], token_places, KEY_VALUE_HEADS)
        value_rows = kv_rows[:, kv_width:].astype(jnp.bfloat16)
        seg_row = jnp.zeros((8, 2 * kv_width), jnp.bfloat16)
        seg_row = seg_row.at[0, :token_slots].set(qseg.astype(jnp.bfloat16))
        own_block = jnp.concatenate(
            [jnp.concatenate([key_norm, value_rows], axis=1), seg_row], axis=0
        )
        query_weights = lax.all_gather(query_weight, "dp", axis=0, tiled=True)
        own_block, query_weights = lax.optimization_barrier((own_block, query_weights))
        query = jnp.dot(inputs, query_weights, preferred_element_type=jnp.float32)
        gathered = lax.all_gather(own_block, "ctx", axis=0, tiled=True).reshape(
            shards, token_slots + 8, 2 * kv_width
        )
        key_count = shards * token_slots
        key_portion = gathered[:, :token_slots, :kv_width].reshape(
            key_count, KEY_VALUE_HEADS, HEAD_SIZE
        )
        value_portion = gathered[:, :token_slots, kv_width:].reshape(
            key_count, KEY_VALUE_HEADS, HEAD_SIZE
        )
        kseg = gathered[:, token_slots, :token_slots].reshape(key_count).astype(jnp.int32)
        kpos = (starts[:, None] + offsets[None, :]).reshape(key_count)
        klive = (offsets[None, :] < counts[:, None]).reshape(key_count)
        kchunk = (kpos + STRETCH - cstart) // STRETCH

        query_norm = rotary_then_norm(query, token_places, QUERY_HEADS)
        head_group = QUERY_HEADS // KEY_VALUE_HEADS
        per_head_queries = query_norm.reshape(token_slots, KEY_VALUE_HEADS, head_group, HEAD_SIZE)

        scores = jnp.einsum(
            "qhgd,khd->hgqk",
            per_head_queries,
            key_portion,
            preferred_element_type=jnp.float32,
        ) * (1.0 / math.sqrt(HEAD_SIZE))
        allowed = (kseg[None, :] == qseg[:, None]) & (kchunk[None, :] == qchunk[:, None])
        allowed = allowed & klive[None, :] & (kpos[None, :] <= token_places[:, None])
        weights = jnp.where(allowed[None, None], jnp.exp(scores), 0.0)
        denom = jnp.sum(weights, axis=-1)
        numer = jnp.einsum(
            "hgqk,khd->qhgd",
            weights.astype(jnp.bfloat16),
            value_portion,
            preferred_element_type=jnp.float32,
        )

        denom_rows = jnp.transpose(denom, (2, 0, 1))
        safe = jnp.where(live[:, None, None], denom_rows, 1.0)
        result = numer / safe[..., None] * live[:, None, None, None].astype(jnp.float32)
        attention = result.reshape(token_slots, QUERY_HEADS * HEAD_SIZE).astype(jnp.bfloat16)
        verdict = jnp.dot(attention, score_vector, preferred_element_type=jnp.float32)
        loglik = jax.nn.log_sigmoid(verdict)
        onehot = span_ids[0][:, None] == jnp.arange(CAND, dtype=jnp.int32)[None, :]
        sums = jnp.sum(jnp.where(onehot, loglik[:, None], 0.0), axis=0)
        tally = jnp.sum(onehot.astype(jnp.float32), axis=0)
        total = jnp.concatenate([sums, tally])
        bit = 1
        while bit < shards:
            pairs = [(s, s ^ bit) for s in range(shards)]
            total = total + lax.ppermute(total, "ctx", pairs)
            bit *= 2
        return (attention[None], (total[:CAND] / total[CAND:])[None])

    return per_device


def solution(mesh):
    placed = (
        P("dp", "ctx", None),
        P("dp", None),
        P("dp"),
        P("dp", "ctx"),
        P("dp", "ctx"),
        P("dp", None),
        P("dp", None),
        P("dp", None),
        P(),
    )
    return jax.shard_map(
        make_per_device(mesh.shape["ctx"]),
        mesh=mesh,
        in_specs=placed,
        out_specs=(P("dp", "ctx", None), P("dp", None)),
        check_vma=False,
    )
```

```python
import math

import jax
import jax.numpy as jnp
from jax import lax
from jax.sharding import Mesh, PartitionSpec as P

QUERY_HEADS = 20
KEY_VALUE_HEADS = 4
HEAD_SIZE = 128
STRETCH = 8192
CAND = 32


THETA = 500000.0
EPS = 1e-05


def rotary_then_norm(value_rows, token_places, heads):
    token_count = value_rows.shape[0]
    half = HEAD_SIZE // 2
    shaped = value_rows.reshape(token_count, heads, HEAD_SIZE)
    freqs = jnp.exp(jnp.arange(half, dtype=jnp.float32) * (-2.0 * math.log(THETA) / HEAD_SIZE))
    angles = token_places.astype(jnp.float32)[:, None] * freqs[None, :]
    cosine = jnp.cos(angles)[:, None, :]
    sine = jnp.sin(angles)[:, None, :]
    leading_block = shaped[..., :half]
    second = shaped[..., half:]
    turned = jnp.concatenate(
        [leading_block * cosine - second * sine, second * cosine + leading_block * sine], axis=-1
    )
    scale = lax.rsqrt(jnp.mean(turned * turned, axis=-1, keepdims=True) + EPS)
    return (turned * scale).astype(jnp.bfloat16).reshape(token_count, heads * HEAD_SIZE)


def make_per_device(shards, inner):
    def per_device(
        tokens,
        shard_counts,
        stretch_start,
        segment_ids,
        span_ids,
        query_weight,
        key_matrix,
        value_matrix,
        score_vector,
    ):
        inputs = tokens[0]
        token_slots = inputs.shape[0]
        kv_width = KEY_VALUE_HEADS * HEAD_SIZE
        mine = lax.axis_index("cx") * inner + lax.axis_index("cz")
        counts = shard_counts[0]
        starts = jnp.cumsum(counts) - counts
        offsets = jnp.arange(token_slots, dtype=jnp.int32)
        token_places = starts[mine] + offsets
        live = offsets < counts[mine]
        cstart = stretch_start[0]
        qseg = segment_ids[0]
        qchunk = (token_places + STRETCH - cstart) // STRETCH

        kv_weights = lax.all_gather(
            jnp.concatenate([key_matrix, value_matrix], axis=1), "dp", axis=0, tiled=True
        )
        kv_rows = jnp.dot(inputs, kv_weights, preferred_element_type=jnp.float32)
        key_norm = rotary_then_norm(kv_rows[:, :kv_width], token_places, KEY_VALUE_HEADS)
        value_rows = kv_rows[:, kv_width:].astype(jnp.bfloat16)
        seg_row = jnp.zeros((8, 2 * kv_width), jnp.bfloat16)
        seg_row = seg_row.at[0, :token_slots].set(qseg.astype(jnp.bfloat16))
        own_block = jnp.concatenate(
            [jnp.concatenate([key_norm, value_rows], axis=1), seg_row], axis=0
        )
        query_weights = lax.all_gather(query_weight, "dp", axis=0, tiled=True)
        own_block, query_weights = lax.optimization_barrier((own_block, query_weights))
        query = jnp.dot(inputs, query_weights, preferred_element_type=jnp.float32)
        gathered = lax.all_gather(own_block, "cz", axis=0, tiled=True)
        gathered = lax.all_gather(gathered, "cx", axis=0, tiled=True).reshape(
            shards, token_slots + 8, 2 * kv_width
        )
        key_count = shards * token_slots
        key_portion = gathered[:, :token_slots, :kv_width].reshape(
            key_count, KEY_VALUE_HEADS, HEAD_SIZE
        )
        value_portion = gathered[:, :token_slots, kv_width:].reshape(
            key_count, KEY_VALUE_HEADS, HEAD_SIZE
        )
        kseg = gathered[:, token_slots, :token_slots].reshape(key_count).astype(jnp.int32)
        kpos = (starts[:, None] + offsets[None, :]).reshape(key_count)
        klive = (offsets[None, :] < counts[:, None]).reshape(key_count)
        kchunk = (kpos + STRETCH - cstart) // STRETCH

        query_norm = rotary_then_norm(query, token_places, QUERY_HEADS)
        head_group = QUERY_HEADS // KEY_VALUE_HEADS
        per_head_queries = query_norm.reshape(token_slots, KEY_VALUE_HEADS, head_group, HEAD_SIZE)

        scores = jnp.einsum(
            "qhgd,khd->hgqk",
            per_head_queries,
            key_portion,
            preferred_element_type=jnp.float32,
        ) * (1.0 / math.sqrt(HEAD_SIZE))
        allowed = (kseg[None, :] == qseg[:, None]) & (kchunk[None, :] == qchunk[:, None])
        allowed = allowed & klive[None, :] & (kpos[None, :] <= token_places[:, None])
        weights = jnp.where(allowed[None, None], jnp.exp(scores), 0.0)
        denom = jnp.sum(weights, axis=-1)
        numer = jnp.einsum(
            "hgqk,khd->qhgd",
            weights.astype(jnp.bfloat16),
            value_portion,
            preferred_element_type=jnp.float32,
        )

        denom_rows = jnp.transpose(denom, (2, 0, 1))
        safe = jnp.where(live[:, None, None], denom_rows, 1.0)
        result = numer / safe[..., None] * live[:, None, None, None].astype(jnp.float32)
        attention = result.reshape(token_slots, QUERY_HEADS * HEAD_SIZE).astype(jnp.bfloat16)
        verdict = jnp.dot(attention, score_vector, preferred_element_type=jnp.float32)
        loglik = jax.nn.log_sigmoid(verdict)
        onehot = span_ids[0][:, None] == jnp.arange(CAND, dtype=jnp.int32)[None, :]
        sums = jnp.sum(jnp.where(onehot, loglik[:, None], 0.0), axis=0)
        tally = jnp.sum(onehot.astype(jnp.float32), axis=0)
        total = jnp.concatenate([sums, tally])
        for axis, size in (("cz", inner), ("cx", shards // inner)):
            bit = 1
            while bit < size:
                pairs = [(s, s ^ bit) for s in range(size)]
                total = total + lax.ppermute(total, axis, pairs)
                bit *= 2
        return (attention[None], (total[:CAND] / total[CAND:])[None])

    return per_device


def solution(mesh):
    shards = mesh.shape["ctx"]
    inner = 4 if shards % 4 == 0 else 1
    split = Mesh(
        mesh.devices.reshape(mesh.shape["dp"], shards // inner, inner), ("dp", "cx", "cz")
    )
    ctx = ("cx", "cz")
    placed = (
        P("dp", ctx, None),
        P("dp", None),
        P("dp"),
        P("dp", ctx),
        P("dp", ctx),
        P("dp", None),
        P("dp", None),
        P("dp", None),
        P(),
    )
    return jax.shard_map(
        make_per_device(shards, inner),
        mesh=split,
        in_specs=placed,
        out_specs=(P("dp", ctx, None), P("dp", None)),
        check_vma=False,
    )
```

```python
import math

import jax
import jax.numpy as jnp
from jax import lax
from jax.sharding import Mesh, PartitionSpec as P

QUERY_HEADS = 20
KEY_VALUE_HEADS = 4
HEAD_SIZE = 128
STRETCH = 8192
CAND = 32


THETA = 500000.0
EPS = 1e-05


def rotary_then_norm(value_rows, token_places, heads):
    token_count = value_rows.shape[0]
    half = HEAD_SIZE // 2
    shaped = value_rows.reshape(token_count, heads, HEAD_SIZE)
    freqs = jnp.exp(jnp.arange(half, dtype=jnp.float32) * (-2.0 * math.log(THETA) / HEAD_SIZE))
    angles = token_places.astype(jnp.float32)[:, None] * freqs[None, :]
    cosine = jnp.cos(angles)[:, None, :]
    sine = jnp.sin(angles)[:, None, :]
    leading_block = shaped[..., :half]
    second = shaped[..., half:]
    turned = jnp.concatenate(
        [leading_block * cosine - second * sine, second * cosine + leading_block * sine], axis=-1
    )
    scale = lax.rsqrt(jnp.mean(turned * turned, axis=-1, keepdims=True) + EPS)
    return (turned * scale).astype(jnp.bfloat16).reshape(token_count, heads * HEAD_SIZE)


def make_per_device(shards, inner):
    def per_device(
        tokens,
        shard_counts,
        stretch_start,
        segment_ids,
        span_ids,
        query_weight,
        key_matrix,
        value_matrix,
        score_vector,
    ):
        inputs = tokens[0]
        token_slots = inputs.shape[0]
        kv_width = KEY_VALUE_HEADS * HEAD_SIZE
        mine = lax.axis_index("cx") * inner + lax.axis_index("cz")
        counts = shard_counts[0]
        starts = jnp.cumsum(counts) - counts
        offsets = jnp.arange(token_slots, dtype=jnp.int32)
        token_places = starts[mine] + offsets
        live = offsets < counts[mine]
        cstart = stretch_start[0]
        qseg = segment_ids[0]
        qchunk = (token_places + STRETCH - cstart) // STRETCH

        q_width = QUERY_HEADS * HEAD_SIZE
        core = lax.axis_index("dc")
        swap = [(0, 1), (1, 0)]
        weights_local = jnp.concatenate([query_weight, key_matrix, value_matrix], axis=1)
        half = weights_local.shape[1] // 2
        chunk = weights_local.shape[0]
        mine_half = lax.dynamic_slice_in_dim(weights_local, core * half, half, axis=1)
        other_half = lax.dynamic_slice_in_dim(weights_local, (1 - core) * half, half, axis=1)
        partner_rows = lax.ppermute(other_half, "dc", swap)
        partner_tokens = lax.ppermute(inputs, "dc", swap)
        rows_block = jnp.concatenate([mine_half, partner_rows], axis=0)
        half_weights = lax.all_gather(rows_block, ("dz", "dy"), axis=0, tiled=True)
        both = jnp.concatenate([inputs, partner_tokens], axis=0)
        features = both.shape[1]
        paired = both.reshape(2 * token_slots, features // (2 * chunk), 2, chunk)
        paired = jnp.where(core == 0, paired, paired[:, :, ::-1, :])
        both = paired.reshape(2 * token_slots, features)
        projected = jnp.dot(both, half_weights, preferred_element_type=jnp.float32)
        returned = lax.ppermute(projected[token_slots:], "dc", swap)
        own_part = projected[:token_slots]
        full = jnp.where(
            core == 0,
            jnp.concatenate([own_part, returned], axis=1),
            jnp.concatenate([returned, own_part], axis=1),
        )
        query = full[:, :q_width]
        key_norm = rotary_then_norm(full[:, q_width : q_width + kv_width], token_places, KEY_VALUE_HEADS)
        value_rows = full[:, q_width + kv_width :].astype(jnp.bfloat16)
        seg_row = jnp.zeros((8, 2 * kv_width), jnp.bfloat16)
        seg_row = seg_row.at[0, :token_slots].set(qseg.astype(jnp.bfloat16))
        own_block = jnp.concatenate(
            [jnp.concatenate([key_norm, value_rows], axis=1), seg_row], axis=0
        )
        gathered = lax.all_gather(own_block, ("cx", "cz"), axis=0, tiled=True).reshape(
            shards, token_slots + 8, 2 * kv_width
        )
        key_count = shards * token_slots
        key_portion = gathered[:, :token_slots, :kv_width].reshape(
            key_count, KEY_VALUE_HEADS, HEAD_SIZE
        )
        value_portion = gathered[:, :token_slots, kv_width:].reshape(
            key_count, KEY_VALUE_HEADS, HEAD_SIZE
        )
        kseg = gathered[:, token_slots, :token_slots].reshape(key_count).astype(jnp.int32)
        kpos = (starts[:, None] + offsets[None, :]).reshape(key_count)
        klive = (offsets[None, :] < counts[:, None]).reshape(key_count)
        kchunk = (kpos + STRETCH - cstart) // STRETCH

        query_norm = rotary_then_norm(query, token_places, QUERY_HEADS)
        head_group = QUERY_HEADS // KEY_VALUE_HEADS
        per_head_queries = query_norm.reshape(token_slots, KEY_VALUE_HEADS, head_group, HEAD_SIZE)

        scores = jnp.einsum(
            "qhgd,khd->hgqk",
            per_head_queries,
            key_portion,
            preferred_element_type=jnp.float32,
        ) * (1.0 / math.sqrt(HEAD_SIZE))
        allowed = (kseg[None, :] == qseg[:, None]) & (kchunk[None, :] == qchunk[:, None])
        allowed = allowed & klive[None, :] & (kpos[None, :] <= token_places[:, None])
        weights = jnp.where(allowed[None, None], jnp.exp(scores), 0.0)
        denom = jnp.sum(weights, axis=-1)
        numer = jnp.einsum(
            "hgqk,khd->qhgd",
            weights.astype(jnp.bfloat16),
            value_portion,
            preferred_element_type=jnp.float32,
        )

        denom_rows = jnp.transpose(denom, (2, 0, 1))
        safe = jnp.where(live[:, None, None], denom_rows, 1.0)
        result = numer / safe[..., None] * live[:, None, None, None].astype(jnp.float32)
        attention = result.reshape(token_slots, QUERY_HEADS * HEAD_SIZE).astype(jnp.bfloat16)
        verdict = jnp.dot(attention, score_vector, preferred_element_type=jnp.float32)
        loglik = jax.nn.log_sigmoid(verdict)
        onehot = span_ids[0][:, None] == jnp.arange(CAND, dtype=jnp.int32)[None, :]
        sums = jnp.sum(jnp.where(onehot, loglik[:, None], 0.0), axis=0)
        tally = jnp.sum(onehot.astype(jnp.float32), axis=0)
        total = jnp.concatenate([sums, tally])
        for axis, size in (("cz", inner), ("cx", shards // inner)):
            bit = 1
            while bit < size:
                pairs = [(s, s ^ bit) for s in range(size)]
                total = total + lax.ppermute(total, axis, pairs)
                bit *= 2
        return (attention[None], (total[:CAND] / total[CAND:])[None])

    return per_device


def solution(mesh):
    shards = mesh.shape["ctx"]
    inner = 4
    split = Mesh(
        mesh.devices.reshape(2, mesh.shape["dp"] // 4, 2, shards // inner, inner),
        ("dz", "dy", "dc", "cx", "cz"),
    )
    dp = ("dz", "dy", "dc")
    ctx = ("cx", "cz")
    placed = (
        P(dp, ctx, None),
        P(dp, None),
        P(dp),
        P(dp, ctx),
        P(dp, ctx),
        P(dp, None),
        P(dp, None),
        P(dp, None),
        P(),
    )
    return jax.shard_map(
        make_per_device(shards, inner),
        mesh=split,
        in_specs=placed,
        out_specs=(P(dp, ctx, None), P(dp, None)),
        check_vma=False,
    )
```

```python
import math

import jax
import jax.numpy as jnp
from jax import lax
from jax.sharding import Mesh, PartitionSpec as P

QUERY_HEADS = 20
KEY_VALUE_HEADS = 4
HEAD_SIZE = 128
STRETCH = 8192
CAND = 32


THETA = 500000.0
EPS = 1e-05


def rotary_then_norm(value_rows, token_places, heads):
    token_count = value_rows.shape[0]
    half = HEAD_SIZE // 2
    shaped = value_rows.reshape(token_count, heads, HEAD_SIZE)
    freqs = jnp.exp(jnp.arange(half, dtype=jnp.float32) * (-2.0 * math.log(THETA) / HEAD_SIZE))
    angles = token_places.astype(jnp.float32)[:, None] * freqs[None, :]
    cosine = jnp.cos(angles)[:, None, :]
    sine = jnp.sin(angles)[:, None, :]
    leading_block = shaped[..., :half]
    second = shaped[..., half:]
    turned = jnp.concatenate(
        [leading_block * cosine - second * sine, second * cosine + leading_block * sine], axis=-1
    )
    scale = lax.rsqrt(jnp.mean(turned * turned, axis=-1, keepdims=True) + EPS)
    return (turned * scale).astype(jnp.bfloat16).reshape(token_count, heads * HEAD_SIZE)


def make_per_device(shards, inner):
    def per_device(
        tokens,
        shard_counts,
        stretch_start,
        segment_ids,
        span_ids,
        query_weight,
        key_matrix,
        value_matrix,
        score_vector,
    ):
        inputs = tokens[0]
        token_slots = inputs.shape[0]
        kv_width = KEY_VALUE_HEADS * HEAD_SIZE
        mine = lax.axis_index("cx") * inner + lax.axis_index("cz")
        counts = shard_counts[0]
        starts = jnp.cumsum(counts) - counts
        offsets = jnp.arange(token_slots, dtype=jnp.int32)
        token_places = starts[mine] + offsets
        live = offsets < counts[mine]
        cstart = stretch_start[0]
        qseg = segment_ids[0]
        qchunk = (token_places + STRETCH - cstart) // STRETCH

        q_width = QUERY_HEADS * HEAD_SIZE
        core = lax.axis_index("dc")
        swap = [(0, 1), (1, 0)]
        weights_local = jnp.concatenate([query_weight, key_matrix, value_matrix], axis=1)
        half = weights_local.shape[1] // 2
        chunk = weights_local.shape[0]
        mine_half = lax.dynamic_slice_in_dim(weights_local, core * half, half, axis=1)
        other_half = lax.dynamic_slice_in_dim(weights_local, (1 - core) * half, half, axis=1)
        partner_rows = lax.ppermute(other_half, "dc", swap)
        partner_tokens = lax.ppermute(inputs, "dc", swap)
        rows_block = jnp.concatenate([mine_half, partner_rows], axis=0)
        half_weights = lax.all_gather(rows_block, ("dz", "dy"), axis=0, tiled=True)
        both = jnp.concatenate([inputs, partner_tokens], axis=0)
        features = both.shape[1]
        paired = both.reshape(2 * token_slots, features // (2 * chunk), 2, chunk)
        paired = jnp.where(core == 0, paired, paired[:, :, ::-1, :])
        both = paired.reshape(2 * token_slots, features)
        projected = jnp.dot(both, half_weights, preferred_element_type=jnp.float32)
        returned = lax.ppermute(projected[token_slots:], "dc", swap)
        own_part = projected[:token_slots]
        full = jnp.where(
            core == 0,
            jnp.concatenate([own_part, returned], axis=1),
            jnp.concatenate([returned, own_part], axis=1),
        )
        query = full[:, :q_width]
        key_norm = rotary_then_norm(full[:, q_width : q_width + kv_width], token_places, KEY_VALUE_HEADS)
        value_rows = full[:, q_width + kv_width :].astype(jnp.bfloat16)
        seg_row = jnp.zeros((8, 2 * kv_width), jnp.bfloat16)
        seg_row = seg_row.at[0, :token_slots].set(qseg.astype(jnp.bfloat16))
        own_block = jnp.concatenate(
            [jnp.concatenate([key_norm, value_rows], axis=1), seg_row], axis=0
        )
        gathered = lax.all_gather(own_block, ("cx", "cz"), axis=0, tiled=True).reshape(
            shards, token_slots + 8, 2 * kv_width
        )
        key_count = shards * token_slots
        key_portion = gathered[:, :token_slots, :kv_width].reshape(
            key_count, KEY_VALUE_HEADS, HEAD_SIZE
        )
        value_portion = gathered[:, :token_slots, kv_width:].reshape(
            key_count, KEY_VALUE_HEADS, HEAD_SIZE
        )
        kseg = gathered[:, token_slots, :token_slots].reshape(key_count).astype(jnp.int32)
        kpos = (starts[:, None] + offsets[None, :]).reshape(key_count)
        klive = (offsets[None, :] < counts[:, None]).reshape(key_count)
        kchunk = (kpos + STRETCH - cstart) // STRETCH

        query_norm = rotary_then_norm(query, token_places, QUERY_HEADS)
        head_group = QUERY_HEADS // KEY_VALUE_HEADS
        per_head_queries = query_norm.reshape(token_slots, KEY_VALUE_HEADS, head_group, HEAD_SIZE)

        scores = jnp.einsum(
            "qhgd,khd->hgqk",
            per_head_queries,
            key_portion,
            preferred_element_type=jnp.float32,
        ) * (1.0 / math.sqrt(HEAD_SIZE))
        allowed = (kseg[None, :] == qseg[:, None]) & (kchunk[None, :] == qchunk[:, None])
        allowed = allowed & klive[None, :] & (kpos[None, :] <= token_places[:, None])
        weights = jnp.where(allowed[None, None], jnp.exp(scores), 0.0)
        denom = jnp.sum(weights, axis=-1)
        numer = jnp.einsum(
            "hgqk,khd->qhgd",
            weights.astype(jnp.bfloat16),
            value_portion,
            preferred_element_type=jnp.float32,
        )

        denom_rows = jnp.transpose(denom, (2, 0, 1))
        safe = jnp.where(live[:, None, None], denom_rows, 1.0)
        result = numer / safe[..., None] * live[:, None, None, None].astype(jnp.float32)
        attention = result.reshape(token_slots, QUERY_HEADS * HEAD_SIZE).astype(jnp.bfloat16)
        verdict = jnp.dot(attention, score_vector, preferred_element_type=jnp.float32)
        loglik = jax.nn.log_sigmoid(verdict)
        onehot = span_ids[0][:, None] == jnp.arange(CAND, dtype=jnp.int32)[None, :]
        sums = jnp.sum(jnp.where(onehot, loglik[:, None], 0.0), axis=0)
        tally = jnp.sum(onehot.astype(jnp.float32), axis=0)
        total = jnp.concatenate([sums, tally])
        for axis, size in (("cz", inner), ("cx", shards // inner)):
            here = lax.axis_index(axis)
            parts = [total]
            for shift in range(1, size):
                pairs = [(s, (s + shift) % size) for s in range(size)]
                parts.append(lax.ppermute(total, axis, pairs))
            order = (here - jnp.arange(size, dtype=jnp.int32)) % size
            by_source = jnp.take(jnp.stack(parts), order, axis=0)
            total = by_source[0]
            for s in range(1, size):
                total = total + by_source[s]
        return (attention[None], (total[:CAND] / total[CAND:])[None])

    return per_device


def solution(mesh):
    shards = mesh.shape["ctx"]
    inner = 4
    split = Mesh(
        mesh.devices.reshape(2, mesh.shape["dp"] // 4, 2, shards // inner, inner),
        ("dz", "dy", "dc", "cx", "cz"),
    )
    dp = ("dz", "dy", "dc")
    ctx = ("cx", "cz")
    placed = (
        P(dp, ctx, None),
        P(dp, None),
        P(dp),
        P(dp, ctx),
        P(dp, ctx),
        P(dp, None),
        P(dp, None),
        P(dp, None),
        P(),
    )
    return jax.shard_map(
        make_per_device(shards, inner),
        mesh=split,
        in_specs=placed,
        out_specs=(P(dp, ctx, None), P(dp, None)),
        check_vma=False,
    )
```

```python
import math

import jax
import jax.numpy as jnp
from jax import lax
from jax.sharding import Mesh, PartitionSpec as P

QUERY_HEADS = 20
KEY_VALUE_HEADS = 4
HEAD_SIZE = 128
STRETCH = 8192
CAND = 32


THETA = 500000.0
EPS = 1e-05


def rotary_then_norm(value_rows, token_places, heads):
    token_count = value_rows.shape[0]
    half = HEAD_SIZE // 2
    shaped = value_rows.reshape(token_count, heads, HEAD_SIZE)
    freqs = jnp.exp(jnp.arange(half, dtype=jnp.float32) * (-2.0 * math.log(THETA) / HEAD_SIZE))
    angles = token_places.astype(jnp.float32)[:, None] * freqs[None, :]
    cosine = jnp.cos(angles)[:, None, :]
    sine = jnp.sin(angles)[:, None, :]
    leading_block = shaped[..., :half]
    second = shaped[..., half:]
    turned = jnp.concatenate(
        [leading_block * cosine - second * sine, second * cosine + leading_block * sine], axis=-1
    )
    scale = lax.rsqrt(jnp.mean(turned * turned, axis=-1, keepdims=True) + EPS)
    return (turned * scale).astype(jnp.bfloat16).reshape(token_count, heads * HEAD_SIZE)


def make_per_device(shards, inner, dp_size):
    def per_device(
        tokens,
        shard_counts,
        stretch_start,
        segment_ids,
        span_ids,
        query_weight,
        key_matrix,
        value_matrix,
        score_vector,
    ):
        inputs = tokens[0]
        token_slots = inputs.shape[0]
        kv_width = KEY_VALUE_HEADS * HEAD_SIZE
        mine = lax.axis_index("cx") * inner + lax.axis_index("cz")
        counts = shard_counts[0]
        starts = jnp.cumsum(counts) - counts
        offsets = jnp.arange(token_slots, dtype=jnp.int32)
        token_places = starts[mine] + offsets
        live = offsets < counts[mine]
        cstart = stretch_start[0]
        qseg = segment_ids[0]
        qchunk = (token_places + STRETCH - cstart) // STRETCH

        q_width = QUERY_HEADS * HEAD_SIZE
        core = lax.axis_index("dc")
        swap = [(0, 1), (1, 0)]
        weights_local = jnp.concatenate([query_weight, key_matrix, value_matrix], axis=1)
        half = weights_local.shape[1] // 2
        chunk = weights_local.shape[0]
        mine_half = lax.dynamic_slice_in_dim(weights_local, core * half, half, axis=1)
        other_half = lax.dynamic_slice_in_dim(weights_local, (1 - core) * half, half, axis=1)
        partner_rows = lax.ppermute(other_half, "dc", swap)
        partner_tokens = lax.ppermute(inputs, "dc", swap)
        rows_block = jnp.concatenate([mine_half, partner_rows], axis=0)
        chips = dp_size // 2
        received = [rows_block]
        for shift in range(1, chips):
            pairs = [(s, (s + shift) % chips) for s in range(chips)]
            received.append(lax.ppermute(rows_block, ("dz", "dy"), pairs))
        half_weights = jnp.concatenate(received, axis=0)
        chip = lax.axis_index(("dz", "dy"))
        both = jnp.concatenate([inputs, partner_tokens], axis=0)
        features = both.shape[1]
        paired = both.reshape(2 * token_slots, chips, 2, chunk)
        paired = jnp.where(core == 0, paired, paired[:, :, ::-1, :])
        sources = (chip - jnp.arange(chips, dtype=jnp.int32)) % chips
        paired = jnp.take(paired, sources, axis=1)
        both = paired.reshape(2 * token_slots, features)
        projected = jnp.dot(both, half_weights, preferred_element_type=jnp.float32)
        returned = lax.ppermute(projected[token_slots:], "dc", swap)
        own_part = projected[:token_slots]
        full = jnp.where(
            core == 0,
            jnp.concatenate([own_part, returned], axis=1),
            jnp.concatenate([returned, own_part], axis=1),
        )
        query = full[:, :q_width]
        key_norm = rotary_then_norm(full[:, q_width : q_width + kv_width], token_places, KEY_VALUE_HEADS)
        value_rows = full[:, q_width + kv_width :].astype(jnp.bfloat16)
        seg_row = jnp.zeros((8, 2 * kv_width), jnp.bfloat16)
        seg_row = seg_row.at[0, :token_slots].set(qseg.astype(jnp.bfloat16))
        own_block = jnp.concatenate(
            [jnp.concatenate([key_norm, value_rows], axis=1), seg_row], axis=0
        )
        gathered = lax.all_gather(own_block, ("cx", "cz"), axis=0, tiled=True).reshape(
            shards, token_slots + 8, 2 * kv_width
        )
        key_count = shards * token_slots
        key_portion = gathered[:, :token_slots, :kv_width].reshape(
            key_count, KEY_VALUE_HEADS, HEAD_SIZE
        )
        value_portion = gathered[:, :token_slots, kv_width:].reshape(
            key_count, KEY_VALUE_HEADS, HEAD_SIZE
        )
        kseg = gathered[:, token_slots, :token_slots].reshape(key_count).astype(jnp.int32)
        kpos = (starts[:, None] + offsets[None, :]).reshape(key_count)
        klive = (offsets[None, :] < counts[:, None]).reshape(key_count)
        kchunk = (kpos + STRETCH - cstart) // STRETCH

        query_norm = rotary_then_norm(query, token_places, QUERY_HEADS)
        head_group = QUERY_HEADS // KEY_VALUE_HEADS
        per_head_queries = query_norm.reshape(token_slots, KEY_VALUE_HEADS, head_group, HEAD_SIZE)

        scores = jnp.einsum(
            "qhgd,khd->hgqk",
            per_head_queries,
            key_portion,
            preferred_element_type=jnp.float32,
        ) * (1.0 / math.sqrt(HEAD_SIZE))
        allowed = (kseg[None, :] == qseg[:, None]) & (kchunk[None, :] == qchunk[:, None])
        allowed = allowed & klive[None, :] & (kpos[None, :] <= token_places[:, None])
        weights = jnp.where(allowed[None, None], jnp.exp(scores), 0.0)
        denom = jnp.sum(weights, axis=-1)
        numer = jnp.einsum(
            "hgqk,khd->qhgd",
            weights.astype(jnp.bfloat16),
            value_portion,
            preferred_element_type=jnp.float32,
        )

        denom_rows = jnp.transpose(denom, (2, 0, 1))
        safe = jnp.where(live[:, None, None], denom_rows, 1.0)
        result = numer / safe[..., None] * live[:, None, None, None].astype(jnp.float32)
        attention = result.reshape(token_slots, QUERY_HEADS * HEAD_SIZE).astype(jnp.bfloat16)
        verdict = jnp.dot(attention, score_vector, preferred_element_type=jnp.float32)
        loglik = jax.nn.log_sigmoid(verdict)
        onehot = span_ids[0][:, None] == jnp.arange(CAND, dtype=jnp.int32)[None, :]
        sums = jnp.sum(jnp.where(onehot, loglik[:, None], 0.0), axis=0)
        tally = jnp.sum(onehot.astype(jnp.float32), axis=0)
        total = jnp.concatenate([sums, tally])
        for axis, size in (("cz", inner), ("cx", shards // inner)):
            here = lax.axis_index(axis)
            parts = [total]
            for shift in range(1, size):
                pairs = [(s, (s + shift) % size) for s in range(size)]
                parts.append(lax.ppermute(total, axis, pairs))
            order = (here - jnp.arange(size, dtype=jnp.int32)) % size
            by_source = jnp.take(jnp.stack(parts), order, axis=0)
            total = by_source[0]
            for s in range(1, size):
                total = total + by_source[s]
        return (attention[None], (total[:CAND] / total[CAND:])[None])

    return per_device


def solution(mesh):
    shards = mesh.shape["ctx"]
    inner = 4
    split = Mesh(
        mesh.devices.reshape(2, mesh.shape["dp"] // 4, 2, shards // inner, inner),
        ("dz", "dy", "dc", "cx", "cz"),
    )
    dp = ("dz", "dy", "dc")
    ctx = ("cx", "cz")
    placed = (
        P(dp, ctx, None),
        P(dp, None),
        P(dp),
        P(dp, ctx),
        P(dp, ctx),
        P(dp, None),
        P(dp, None),
        P(dp, None),
        P(),
    )
    return jax.shard_map(
        make_per_device(shards, inner, mesh.shape["dp"]),
        mesh=split,
        in_specs=placed,
        out_specs=(P(dp, ctx, None), P(dp, None)),
        check_vma=False,
    )
```

```python
import math

import jax
import jax.numpy as jnp
from jax import lax
from jax.sharding import Mesh, PartitionSpec as P

QUERY_HEADS = 20
KEY_VALUE_HEADS = 4
HEAD_SIZE = 128
STRETCH = 8192
CAND = 32


THETA = 500000.0
EPS = 1e-05


def rotary_then_norm(value_rows, token_places, heads):
    token_count = value_rows.shape[0]
    half = HEAD_SIZE // 2
    shaped = value_rows.reshape(token_count, heads, HEAD_SIZE)
    freqs = jnp.exp(jnp.arange(half, dtype=jnp.float32) * (-2.0 * math.log(THETA) / HEAD_SIZE))
    angles = token_places.astype(jnp.float32)[:, None] * freqs[None, :]
    cosine = jnp.cos(angles)[:, None, :]
    sine = jnp.sin(angles)[:, None, :]
    leading_block = shaped[..., :half]
    second = shaped[..., half:]
    turned = jnp.concatenate(
        [leading_block * cosine - second * sine, second * cosine + leading_block * sine], axis=-1
    )
    scale = lax.rsqrt(jnp.mean(turned * turned, axis=-1, keepdims=True) + EPS)
    return (turned * scale).astype(jnp.bfloat16).reshape(token_count, heads * HEAD_SIZE)


def ctx_sum(total, shards, inner):
    for axis, size in (("cz", inner), ("cx", shards // inner)):
        here = lax.axis_index(axis)
        parts = [total]
        for shift in range(1, size):
            pairs = [(s, (s + shift) % size) for s in range(size)]
            parts.append(lax.ppermute(total, axis, pairs))
        order = (here - jnp.arange(size, dtype=jnp.int32)) % size
        by_source = jnp.take(jnp.stack(parts), order, axis=0)
        total = by_source[0]
        for s in range(1, size):
            total = total + by_source[s]
    return total


def make_per_device(shards, inner):
    def per_device(
        tokens,
        shard_counts,
        stretch_start,
        segment_ids,
        span_ids,
        query_weight,
        key_matrix,
        value_matrix,
        score_vector,
    ):
        inputs = tokens[0]
        token_slots = inputs.shape[0]
        kv_width = KEY_VALUE_HEADS * HEAD_SIZE
        mine = lax.axis_index("cx") * inner + lax.axis_index("cz")
        counts = shard_counts[0]
        starts = jnp.cumsum(counts) - counts
        offsets = jnp.arange(token_slots, dtype=jnp.int32)
        token_places = starts[mine] + offsets
        live = offsets < counts[mine]
        cstart = stretch_start[0]
        qseg = segment_ids[0]
        qchunk = (token_places + STRETCH - cstart) // STRETCH
        first_count = jnp.sum((live & (qseg == 0)).astype(jnp.int32)).reshape(1)
        doc_edge = ctx_sum(first_count, shards, inner)[0]

        q_width = QUERY_HEADS * HEAD_SIZE
        core = lax.axis_index("dc")
        swap = [(0, 1), (1, 0)]
        weights_local = jnp.concatenate([query_weight, key_matrix, value_matrix], axis=1)
        half = weights_local.shape[1] // 2
        chunk = weights_local.shape[0]
        mine_half = lax.dynamic_slice_in_dim(weights_local, core * half, half, axis=1)
        other_half = lax.dynamic_slice_in_dim(weights_local, (1 - core) * half, half, axis=1)
        partner_rows = lax.ppermute(other_half, "dc", swap)
        partner_tokens = lax.ppermute(inputs, "dc", swap)
        rows_block = jnp.concatenate([mine_half, partner_rows], axis=0)
        half_weights = lax.all_gather(rows_block, ("dz", "dy"), axis=0, tiled=True)
        both = jnp.concatenate([inputs, partner_tokens], axis=0)
        features = both.shape[1]
        paired = both.reshape(2 * token_slots, features // (2 * chunk), 2, chunk)
        paired = jnp.where(core == 0, paired, paired[:, :, ::-1, :])
        both = paired.reshape(2 * token_slots, features)
        projected = jnp.dot(both, half_weights, preferred_element_type=jnp.float32)
        returned = lax.ppermute(projected[token_slots:], "dc", swap)
        own_part = projected[:token_slots]
        full = jnp.where(
            core == 0,
            jnp.concatenate([own_part, returned], axis=1),
            jnp.concatenate([returned, own_part], axis=1),
        )
        query = full[:, :q_width]
        key_norm = rotary_then_norm(full[:, q_width : q_width + kv_width], token_places, KEY_VALUE_HEADS)
        value_rows = full[:, q_width + kv_width :].astype(jnp.bfloat16)
        own_block = jnp.concatenate([key_norm, value_rows], axis=1)
        gathered = lax.all_gather(own_block, ("cx", "cz"), axis=0, tiled=True).reshape(
            shards, token_slots, 2 * kv_width
        )
        key_count = shards * token_slots
        key_portion = gathered[:, :token_slots, :kv_width].reshape(
            key_count, KEY_VALUE_HEADS, HEAD_SIZE
        )
        value_portion = gathered[:, :token_slots, kv_width:].reshape(
            key_count, KEY_VALUE_HEADS, HEAD_SIZE
        )
        kpos = (starts[:, None] + offsets[None, :]).reshape(key_count)
        kseg = (kpos >= doc_edge).astype(jnp.int32)
        klive = (offsets[None, :] < counts[:, None]).reshape(key_count)
        kchunk = (kpos + STRETCH - cstart) // STRETCH

        query_norm = rotary_then_norm(query, token_places, QUERY_HEADS)
        head_group = QUERY_HEADS // KEY_VALUE_HEADS
        per_head_queries = query_norm.reshape(token_slots, KEY_VALUE_HEADS, head_group, HEAD_SIZE)

        scores = jnp.einsum(
            "qhgd,khd->hgqk",
            per_head_queries,
            key_portion,
            preferred_element_type=jnp.float32,
        ) * (1.0 / math.sqrt(HEAD_SIZE))
        allowed = (kseg[None, :] == qseg[:, None]) & (kchunk[None, :] == qchunk[:, None])
        allowed = allowed & klive[None, :] & (kpos[None, :] <= token_places[:, None])
        weights = jnp.where(allowed[None, None], jnp.exp(scores), 0.0)
        denom = jnp.sum(weights, axis=-1)
        numer = jnp.einsum(
            "hgqk,khd->qhgd",
            weights.astype(jnp.bfloat16),
            value_portion,
            preferred_element_type=jnp.float32,
        )

        denom_rows = jnp.transpose(denom, (2, 0, 1))
        safe = jnp.where(live[:, None, None], denom_rows, 1.0)
        result = numer / safe[..., None] * live[:, None, None, None].astype(jnp.float32)
        attention = result.reshape(token_slots, QUERY_HEADS * HEAD_SIZE).astype(jnp.bfloat16)
        verdict = jnp.dot(attention, score_vector, preferred_element_type=jnp.float32)
        loglik = jax.nn.log_sigmoid(verdict)
        onehot = span_ids[0][:, None] == jnp.arange(CAND, dtype=jnp.int32)[None, :]
        sums = jnp.sum(jnp.where(onehot, loglik[:, None], 0.0), axis=0)
        tally = jnp.sum(onehot.astype(jnp.float32), axis=0)
        total = jnp.concatenate([sums, tally])
        total = ctx_sum(total, shards, inner)
        return (attention[None], (total[:CAND] / total[CAND:])[None])

    return per_device


def solution(mesh):
    shards = mesh.shape["ctx"]
    inner = 4
    split = Mesh(
        mesh.devices.reshape(2, mesh.shape["dp"] // 4, 2, shards // inner, inner),
        ("dz", "dy", "dc", "cx", "cz"),
    )
    dp = ("dz", "dy", "dc")
    ctx = ("cx", "cz")
    placed = (
        P(dp, ctx, None),
        P(dp, None),
        P(dp),
        P(dp, ctx),
        P(dp, ctx),
        P(dp, None),
        P(dp, None),
        P(dp, None),
        P(),
    )
    return jax.shard_map(
        make_per_device(shards, inner),
        mesh=split,
        in_specs=placed,
        out_specs=(P(dp, ctx, None), P(dp, None)),
        check_vma=False,
    )
```

```python
import math

import jax
import jax.numpy as jnp
from jax import lax
from jax.sharding import Mesh, PartitionSpec as P

QUERY_HEADS = 20
KEY_VALUE_HEADS = 4
HEAD_SIZE = 128
STRETCH = 8192
CAND = 32


THETA = 500000.0
EPS = 1e-05


def rotary_then_norm(value_rows, token_places, heads):
    token_count = value_rows.shape[0]
    half = HEAD_SIZE // 2
    shaped = value_rows.reshape(token_count, heads, HEAD_SIZE)
    freqs = jnp.exp(jnp.arange(half, dtype=jnp.float32) * (-2.0 * math.log(THETA) / HEAD_SIZE))
    angles = token_places.astype(jnp.float32)[:, None] * freqs[None, :]
    cosine = jnp.cos(angles)[:, None, :]
    sine = jnp.sin(angles)[:, None, :]
    leading_block = shaped[..., :half]
    second = shaped[..., half:]
    turned = jnp.concatenate(
        [leading_block * cosine - second * sine, second * cosine + leading_block * sine], axis=-1
    )
    scale = lax.rsqrt(jnp.mean(turned * turned, axis=-1, keepdims=True) + EPS)
    return (turned * scale).astype(jnp.bfloat16).reshape(token_count, heads * HEAD_SIZE)


def ctx_sum(total, shards, inner):
    for axis, size in (("cz", inner), ("cx", shards // inner)):
        here = lax.axis_index(axis)
        parts = [total]
        for shift in range(1, size):
            pairs = [(s, (s + shift) % size) for s in range(size)]
            parts.append(lax.ppermute(total, axis, pairs))
        order = (here - jnp.arange(size, dtype=jnp.int32)) % size
        by_source = jnp.take(jnp.stack(parts), order, axis=0)
        total = by_source[0]
        for s in range(1, size):
            total = total + by_source[s]
    return total


def make_per_device(shards, inner):
    def per_device(
        tokens,
        shard_counts,
        stretch_start,
        segment_ids,
        span_ids,
        query_weight,
        key_matrix,
        value_matrix,
        score_vector,
    ):
        inputs = tokens[0]
        token_slots = inputs.shape[0]
        kv_width = KEY_VALUE_HEADS * HEAD_SIZE
        mine = lax.axis_index("cx") * inner + lax.axis_index("cz")
        counts = shard_counts[0]
        starts = jnp.cumsum(counts) - counts
        offsets = jnp.arange(token_slots, dtype=jnp.int32)
        token_places = starts[mine] + offsets
        live = offsets < counts[mine]
        cstart = stretch_start[0]
        qseg = segment_ids[0]
        qchunk = (token_places + STRETCH - cstart) // STRETCH
        first_count = jnp.sum((live & (qseg == 0)).astype(jnp.int32)).reshape(1)
        doc_edge = ctx_sum(first_count, shards, inner)[0]

        q_width = QUERY_HEADS * HEAD_SIZE
        core = lax.axis_index("dc")
        swap = [(0, 1), (1, 0)]
        weights_local = jnp.concatenate([query_weight, key_matrix, value_matrix], axis=1)
        half = weights_local.shape[1] // 2
        chunk = weights_local.shape[0]
        mine_half = lax.dynamic_slice_in_dim(weights_local, core * half, half, axis=1)
        other_half = lax.dynamic_slice_in_dim(weights_local, (1 - core) * half, half, axis=1)
        partner_rows = lax.ppermute(other_half, "dc", swap)
        partner_tokens = lax.ppermute(inputs, "dc", swap)
        rows_block = jnp.concatenate([mine_half, partner_rows], axis=0)
        half_weights = lax.all_gather(rows_block, ("dz", "dy"), axis=0, tiled=True)
        both = jnp.concatenate([inputs, partner_tokens], axis=0)
        features = both.shape[1]
        paired = both.reshape(2 * token_slots, features // (2 * chunk), 2, chunk)
        paired = jnp.where(core == 0, paired, paired[:, :, ::-1, :])
        both = paired.reshape(2 * token_slots, features)
        projected = jnp.dot(both, half_weights, preferred_element_type=jnp.float32)
        returned = lax.ppermute(projected[token_slots:], "dc", swap)
        own_part = projected[:token_slots]
        full = jnp.where(
            core == 0,
            jnp.concatenate([own_part, returned], axis=1),
            jnp.concatenate([returned, own_part], axis=1),
        )
        query = full[:, :q_width]
        key_norm = rotary_then_norm(full[:, q_width : q_width + kv_width], token_places, KEY_VALUE_HEADS)
        value_rows = full[:, q_width + kv_width :].astype(jnp.bfloat16)
        key_t = key_norm.reshape(token_slots, KEY_VALUE_HEADS, HEAD_SIZE).transpose(1, 2, 0)
        value_t = value_rows.reshape(token_slots, KEY_VALUE_HEADS, HEAD_SIZE).transpose(1, 2, 0)
        own_block = jnp.concatenate([key_t, value_t], axis=0)
        gathered = lax.all_gather(own_block, ("cx", "cz"), axis=2, tiled=True)
        key_count = shards * token_slots
        key_portion = gathered[:KEY_VALUE_HEADS]
        value_portion = gathered[KEY_VALUE_HEADS:]
        kpos = (starts[:, None] + offsets[None, :]).reshape(key_count)
        kseg = (kpos >= doc_edge).astype(jnp.int32)
        klive = (offsets[None, :] < counts[:, None]).reshape(key_count)
        kchunk = (kpos + STRETCH - cstart) // STRETCH

        query_norm = rotary_then_norm(query, token_places, QUERY_HEADS)
        head_group = QUERY_HEADS // KEY_VALUE_HEADS
        per_head_queries = query_norm.reshape(token_slots, KEY_VALUE_HEADS, head_group, HEAD_SIZE)

        scores = jnp.einsum(
            "qhgd,hdk->hgqk",
            per_head_queries,
            key_portion,
            preferred_element_type=jnp.float32,
        ) * (1.0 / math.sqrt(HEAD_SIZE))
        allowed = (kseg[None, :] == qseg[:, None]) & (kchunk[None, :] == qchunk[:, None])
        allowed = allowed & klive[None, :] & (kpos[None, :] <= token_places[:, None])
        weights = jnp.where(allowed[None, None], jnp.exp(scores), 0.0)
        denom = jnp.sum(weights, axis=-1)
        numer = jnp.einsum(
            "hgqk,hdk->qhgd",
            weights.astype(jnp.bfloat16),
            value_portion,
            preferred_element_type=jnp.float32,
        )

        denom_rows = jnp.transpose(denom, (2, 0, 1))
        safe = jnp.where(live[:, None, None], denom_rows, 1.0)
        result = numer / safe[..., None] * live[:, None, None, None].astype(jnp.float32)
        attention = result.reshape(token_slots, QUERY_HEADS * HEAD_SIZE).astype(jnp.bfloat16)
        verdict = jnp.dot(attention, score_vector, preferred_element_type=jnp.float32)
        loglik = jax.nn.log_sigmoid(verdict)
        onehot = span_ids[0][:, None] == jnp.arange(CAND, dtype=jnp.int32)[None, :]
        sums = jnp.sum(jnp.where(onehot, loglik[:, None], 0.0), axis=0)
        tally = jnp.sum(onehot.astype(jnp.float32), axis=0)
        total = jnp.concatenate([sums, tally])
        total = ctx_sum(total, shards, inner)
        return (attention[None], (total[:CAND] / total[CAND:])[None])

    return per_device


def solution(mesh):
    shards = mesh.shape["ctx"]
    inner = 4
    split = Mesh(
        mesh.devices.reshape(2, mesh.shape["dp"] // 4, 2, shards // inner, inner),
        ("dz", "dy", "dc", "cx", "cz"),
    )
    dp = ("dz", "dy", "dc")
    ctx = ("cx", "cz")
    placed = (
        P(dp, ctx, None),
        P(dp, None),
        P(dp),
        P(dp, ctx),
        P(dp, ctx),
        P(dp, None),
        P(dp, None),
        P(dp, None),
        P(),
    )
    return jax.shard_map(
        make_per_device(shards, inner),
        mesh=split,
        in_specs=placed,
        out_specs=(P(dp, ctx, None), P(dp, None)),
        check_vma=False,
    )
```

```python
import math

import jax
import jax.numpy as jnp
from jax import lax
from jax.sharding import Mesh, PartitionSpec as P

QUERY_HEADS = 20
KEY_VALUE_HEADS = 4
HEAD_SIZE = 128
STRETCH = 8192
CAND = 32


THETA = 500000.0
EPS = 1e-05


def rotary_then_norm(value_rows, token_places, heads):
    token_count = value_rows.shape[0]
    half = HEAD_SIZE // 2
    shaped = value_rows.reshape(token_count, heads, HEAD_SIZE)
    freqs = jnp.exp(jnp.arange(half, dtype=jnp.float32) * (-2.0 * math.log(THETA) / HEAD_SIZE))
    angles = token_places.astype(jnp.float32)[:, None] * freqs[None, :]
    cosine = jnp.cos(angles)[:, None, :]
    sine = jnp.sin(angles)[:, None, :]
    leading_block = shaped[..., :half]
    second = shaped[..., half:]
    turned = jnp.concatenate(
        [leading_block * cosine - second * sine, second * cosine + leading_block * sine], axis=-1
    )
    scale = lax.rsqrt(jnp.mean(turned * turned, axis=-1, keepdims=True) + EPS)
    return (turned * scale).astype(jnp.bfloat16).reshape(token_count, heads * HEAD_SIZE)


def ctx_sum(total, shards, inner):
    for axis, size in (("cz", inner), ("cx", shards // inner)):
        here = lax.axis_index(axis)
        parts = [total]
        for shift in range(1, size):
            pairs = [(s, (s + shift) % size) for s in range(size)]
            parts.append(lax.ppermute(total, axis, pairs))
        order = (here - jnp.arange(size, dtype=jnp.int32)) % size
        by_source = jnp.take(jnp.stack(parts), order, axis=0)
        total = by_source[0]
        for s in range(1, size):
            total = total + by_source[s]
    return total


def make_per_device(shards, inner):
    def per_device(
        tokens,
        shard_counts,
        stretch_start,
        segment_ids,
        span_ids,
        query_weight,
        key_matrix,
        value_matrix,
        score_vector,
    ):
        inputs = tokens[0]
        token_slots = inputs.shape[0]
        kv_width = KEY_VALUE_HEADS * HEAD_SIZE
        mine = lax.axis_index("cx") * inner + lax.axis_index("cz")
        counts = shard_counts[0]
        starts = jnp.cumsum(counts) - counts
        offsets = jnp.arange(token_slots, dtype=jnp.int32)
        token_places = starts[mine] + offsets
        live = offsets < counts[mine]
        cstart = stretch_start[0]
        qseg = segment_ids[0]
        qchunk = (token_places + STRETCH - cstart) // STRETCH
        first_count = jnp.sum((live & (qseg == 0)).astype(jnp.int32)).reshape(1)
        doc_edge = ctx_sum(first_count, shards, inner)[0]

        q_width = QUERY_HEADS * HEAD_SIZE
        core = lax.axis_index("dc")
        swap = [(0, 1), (1, 0)]
        weights_local = jnp.concatenate([key_matrix, value_matrix, query_weight], axis=1)
        half = weights_local.shape[1] // 2
        chunk = weights_local.shape[0]
        mine_half = lax.dynamic_slice_in_dim(weights_local, core * half, half, axis=1)
        other_half = lax.dynamic_slice_in_dim(weights_local, (1 - core) * half, half, axis=1)
        partner_rows = lax.ppermute(other_half, "dc", swap)
        partner_tokens = lax.ppermute(inputs, "dc", swap)
        rows_block = jnp.concatenate([mine_half, partner_rows], axis=0)
        half_weights = lax.all_gather(rows_block, ("dz", "dy"), axis=0, tiled=True)
        both = jnp.concatenate([inputs, partner_tokens], axis=0)
        features = both.shape[1]
        paired = both.reshape(2 * token_slots, features // (2 * chunk), 2, chunk)
        paired = jnp.where(core == 0, paired, paired[:, :, ::-1, :])
        both = paired.reshape(2 * token_slots, features)
        split_at = 2 * kv_width
        projected_kv = jnp.dot(both, half_weights[:, :split_at], preferred_element_type=jnp.float32)
        returned_kv = lax.ppermute(projected_kv[token_slots:], "dc", swap)
        projected_rest = jnp.dot(both, half_weights[:, split_at:], preferred_element_type=jnp.float32)
        returned_rest = lax.ppermute(projected_rest[token_slots:], "dc", swap)
        own_kv = projected_kv[:token_slots]
        own_rest = projected_rest[:token_slots]
        kv_rows = jnp.where(core == 0, own_kv, returned_kv)
        full = jnp.where(
            core == 0,
            jnp.concatenate([own_kv, own_rest, returned_kv, returned_rest], axis=1),
            jnp.concatenate([returned_kv, returned_rest, own_kv, own_rest], axis=1),
        )
        query = full[:, 2 * kv_width :]
        key_norm = rotary_then_norm(kv_rows[:, :kv_width], token_places, KEY_VALUE_HEADS)
        value_rows = kv_rows[:, kv_width:].astype(jnp.bfloat16)
        key_t = key_norm.reshape(token_slots, KEY_VALUE_HEADS, HEAD_SIZE).transpose(1, 2, 0)
        value_t = value_rows.reshape(token_slots, KEY_VALUE_HEADS, HEAD_SIZE).transpose(1, 2, 0)
        own_block = jnp.concatenate([key_t, value_t], axis=0)
        gathered = lax.all_gather(own_block, ("cx", "cz"), axis=2, tiled=True)
        key_count = shards * token_slots
        key_portion = gathered[:KEY_VALUE_HEADS]
        value_portion = gathered[KEY_VALUE_HEADS:]
        kpos = (starts[:, None] + offsets[None, :]).reshape(key_count)
        kseg = (kpos >= doc_edge).astype(jnp.int32)
        klive = (offsets[None, :] < counts[:, None]).reshape(key_count)
        kchunk = (kpos + STRETCH - cstart) // STRETCH

        query_norm = rotary_then_norm(query, token_places, QUERY_HEADS)
        head_group = QUERY_HEADS // KEY_VALUE_HEADS
        per_head_queries = query_norm.reshape(token_slots, KEY_VALUE_HEADS, head_group, HEAD_SIZE)

        scores = jnp.einsum(
            "qhgd,hdk->hgqk",
            per_head_queries,
            key_portion,
            preferred_element_type=jnp.float32,
        ) * (1.0 / math.sqrt(HEAD_SIZE))
        allowed = (kseg[None, :] == qseg[:, None]) & (kchunk[None, :] == qchunk[:, None])
        allowed = allowed & klive[None, :] & (kpos[None, :] <= token_places[:, None])
        weights = jnp.where(allowed[None, None], jnp.exp(scores), 0.0)
        denom = jnp.sum(weights, axis=-1)
        numer = jnp.einsum(
            "hgqk,hdk->qhgd",
            weights.astype(jnp.bfloat16),
            value_portion,
            preferred_element_type=jnp.float32,
        )

        denom_rows = jnp.transpose(denom, (2, 0, 1))
        safe = jnp.where(live[:, None, None], denom_rows, 1.0)
        result = numer / safe[..., None] * live[:, None, None, None].astype(jnp.float32)
        attention = result.reshape(token_slots, QUERY_HEADS * HEAD_SIZE).astype(jnp.bfloat16)
        verdict = jnp.dot(attention, score_vector, preferred_element_type=jnp.float32)
        loglik = jax.nn.log_sigmoid(verdict)
        onehot = span_ids[0][:, None] == jnp.arange(CAND, dtype=jnp.int32)[None, :]
        sums = jnp.sum(jnp.where(onehot, loglik[:, None], 0.0), axis=0)
        tally = jnp.sum(onehot.astype(jnp.float32), axis=0)
        total = jnp.concatenate([sums, tally])
        total = ctx_sum(total, shards, inner)
        return (attention[None], (total[:CAND] / total[CAND:])[None])

    return per_device


def solution(mesh):
    shards = mesh.shape["ctx"]
    inner = 4
    split = Mesh(
        mesh.devices.reshape(2, mesh.shape["dp"] // 4, 2, shards // inner, inner),
        ("dz", "dy", "dc", "cx", "cz"),
    )
    dp = ("dz", "dy", "dc")
    ctx = ("cx", "cz")
    placed = (
        P(dp, ctx, None),
        P(dp, None),
        P(dp),
        P(dp, ctx),
        P(dp, ctx),
        P(dp, None),
        P(dp, None),
        P(dp, None),
        P(),
    )
    return jax.shard_map(
        make_per_device(shards, inner),
        mesh=split,
        in_specs=placed,
        out_specs=(P(dp, ctx, None), P(dp, None)),
        check_vma=False,
    )
```
